256 devices in a mesh: branch: 2 (over z_hi), head: 4 (over x), page: 32 (over y, z_lo, core).
Axes of the slice: x: 4, y: 4, z: 8 (z_hi: 2, z_lo: 4; z = z_hi * 4 + z_lo), core: 2. Of those that a mesh axis runs over, the one named last changes fastest.
Arguments:
- queries: bfloat16 [16384, 4096], P(('branch', 'page'), 'head'), may hold values from -6 to 6
- new_keys: bfloat16 [16384, 512], P(('branch', 'page'), 'head'), may hold values from -6 to 6
- new_values: bfloat16 [16384, 512], P(('branch', 'page'), 'head'), may hold values from -6 to 6
- cache_keys: bfloat16 [128, 64, 512], P(('branch', 'page'), None, 'head'), may hold values from -6 to 6
- cache_values: bfloat16 [128, 64, 512], P(('branch', 'page'), None, 'head'), may hold values from -6 to 6
- block_table: int32 [64, 32], P(('branch', 'page')), may hold values from 0 to 127, as said below
- ancestor_len: int32 [64], P(('branch', 'page')), may hold values from 256 to 2048, as said below
- out_weight: bfloat16 [4096, 8192], P('head', 'page'), may hold values from -0.375 to 0.375
Outputs:
- layer_out: bfloat16 [16384, 8192], P(('branch', 'head'), 'page')
The draws below stay inside these ranges and needn't reach their ends.
Inputs may be any that keep to these rules, and one draw needn't show every extreme that they name: `block_table`: each row names 32 distinct page ids; its first 4 entries are the same for every branch. `ancestor_len`: every branch's ancestors fill its first 4 pages; some branch reaches the maximum.
All inputs are finite; a program needn't handle non-finite values.
Results may differ from the reference program's by a relative error of at most 0.018.
Values may be sent and summed in bfloat16 or wider, within the bound.
No kernel may reach another device: no remote copies, remote signals or barrier semaphores. Data moves between devices by JAX's collectives and lax.ppermute only.
A program may use at most 64 MiB of HBM per device.

```python
import math
import jax
import jax.numpy as jnp
from jax import lax

D = 8192
H = 32
KVH = 4
HD = 128
PAGE_TOK = 64
NEW = 256
BRANCHES = 64
TOKENS = 16384
PAGES = 128
MAXP = 32
ROOT = 4
N_HEAD = 4


def draw_queries(key, part):
    values = jnp.clip(jax.random.normal(jax.random.fold_in(key, 7), (TOKENS, H * HD), jnp.float32), -6.0, 6.0)
    return values.astype(jnp.bfloat16)


def draw_new_keys(key, part):
    values = jnp.clip(jax.random.normal(jax.random.fold_in(key, 8), (TOKENS, KVH * HD), jnp.float32), -6.0, 6.0)
    return values.astype(jnp.bfloat16)


def draw_block_table(key, part):
    order = jax.random.permutation(jax.random.fold_in(key, 11), PAGES)
    shared = order[:ROOT]
    others = order[ROOT:]
    row_keys = jax.random.split(jax.random.fold_in(key, 12), BRANCHES)
    picks = jax.vmap(lambda row_key: jax.random.permutation(row_key, PAGES - ROOT))(row_keys)[:, :MAXP - ROOT]
    table = jnp.concatenate([jnp.broadcast_to(shared[None, :], (BRANCHES, ROOT)), others[picks]], 1)
    return table.astype(jnp.int32)


def draw_ancestor_len(key, part):
    lower = ROOT * PAGE_TOK
    extent = (MAXP - ROOT) * PAGE_TOK
    first_draw = jax.random.randint(jax.random.fold_in(key, 21), (BRANCHES,), 0, extent + 1)
    second_draw = jax.random.randint(jax.random.fold_in(key, 22), (BRANCHES,), 0, extent + 1)
    lengths = lower + first_draw * second_draw // extent
    deepest = jax.random.randint(jax.random.fold_in(key, 23), (), 0, BRANCHES)
    lengths = jnp.where(jnp.arange(BRANCHES) == deepest, MAXP * PAGE_TOK, lengths)
    return lengths.astype(jnp.int32)


def steps_of(stream_key, dims, cuts, least, high):
    factor_of, own = 1.0, jax.random.fold_in(stream_key, 6)
    for axis_at, parts in cuts:
        draws = jnp.exp(jax.random.uniform(jax.random.fold_in(own, axis_at), (parts,), jnp.float32, least / len(cuts), high / len(cuts)))
        factor_of = factor_of * jnp.repeat(draws, dims[axis_at] // parts).reshape([-1 if axis == axis_at else 1 for axis in range(len(dims))])
    return factor_of


def bell_draw(rng, shape, width, limit, shards=(), kind=jnp.bfloat16):
    loudness = steps_of(rng, shape, shards, -0.22, 0.18) if shards else 1.0
    array = jax.random.normal(rng, shape, jnp.float32) * width * loudness
    return jnp.minimum(jnp.maximum(array, -limit), limit).astype(kind)


def setup_inputs(seed: int = 0) -> dict:
    keys = jax.random.split(jax.random.key(seed), 9)
    return {
        "queries": draw_queries(jax.random.fold_in(keys[8], 71), 0),
        "new_keys": draw_new_keys(jax.random.fold_in(keys[8], 71), 0),
        "new_values": bell_draw(keys[2], (TOKENS, KVH * HD), 1.0, 6.0, ((0, 64), (1, 4))),
        "cache_keys": bell_draw(keys[3], (PAGES, PAGE_TOK, KVH * HD), 1.0, 6.0, ((0, 64), (2, 4))),
        "cache_values": bell_draw(keys[4], (PAGES, PAGE_TOK, KVH * HD), 1.0, 6.0, ((0, 64), (2, 4))),
        "block_table": draw_block_table(jax.random.fold_in(keys[8], 71), 0),
        "ancestor_len": draw_ancestor_len(jax.random.fold_in(keys[8], 71), 0),
        "out_weight": bell_draw(keys[7], (H * HD, D), (H * HD // 16) ** -0.5, 0.375, ((0, 4), (1, 32))),
    }


def reference(queries, new_keys, new_values, cache_keys, cache_values, block_table, ancestor_len, out_weight):
    group_size = H // KVH
    score_scale = 1.0 / math.sqrt(HD)
    query_blocks = queries.reshape(BRANCHES, NEW, KVH, group_size, HD)
    key_blocks = new_keys.reshape(BRANCHES, NEW, KVH, HD)
    value_blocks = new_values.reshape(BRANCHES, NEW, KVH, HD)
    cached_k = cache_keys.reshape(PAGES, PAGE_TOK, KVH, HD)
    cached_v = cache_values.reshape(PAGES, PAGE_TOK, KVH, HD)

    def per_branch(branch_data):
        branch_q, branch_k, branch_v, table_row, context = branch_data
        ancestor_k = cached_k[table_row].reshape(MAXP * PAGE_TOK, KVH, HD)
        ancestor_v = cached_v[table_row].reshape(MAXP * PAGE_TOK, KVH, HD)
        all_keys = jnp.concatenate([ancestor_k, branch_k], 0).astype(jnp.float32)
        all_values = jnp.concatenate([ancestor_v, branch_v], 0).astype(jnp.float32)
        positions = jnp.arange(MAXP * PAGE_TOK, dtype=jnp.int32)
        places = jnp.arange(NEW, dtype=jnp.int32)
        ancestor_mask = jnp.broadcast_to((positions < context)[None, :], (NEW, MAXP * PAGE_TOK))
        causal_mask = places[None, :] <= places[:, None]
        key_mask = jnp.concatenate([ancestor_mask, causal_mask], 1)
        scores = jnp.einsum('nkgd,lkd->kgnl', branch_q.astype(jnp.float32), all_keys) * score_scale
        masked = jnp.where(key_mask[None, None], scores, -1e+30)
        row_max = lax.optimization_barrier(jnp.max(masked, axis=-1, keepdims=True))
        numer = jnp.where(key_mask[None, None], jnp.exp(scores - row_max), 0.0).astype(jnp.bfloat16)
        denom = lax.optimization_barrier(jnp.sum(numer.astype(jnp.float32), axis=-1))
        summed = jnp.einsum('kgnl,lkd->nkgd', numer.astype(jnp.float32), all_values)
        attn = summed / jnp.transpose(denom, (2, 0, 1))[..., None]
        return attn.astype(jnp.bfloat16).reshape(NEW, H * HD)
    attn_all = lax.map(per_branch, (query_blocks, key_blocks, value_blocks, block_table, ancestor_len))
    attn_all = attn_all.reshape(TOKENS, H * HD)
    slice_width = H * HD // N_HEAD
    result = jnp.zeros((TOKENS, D), jnp.float32)
    for group_index in range(N_HEAD):
        lower = group_index * slice_width
        partial_term = jnp.dot(attn_all[:, lower:lower + slice_width], out_weight[lower:lower + slice_width], preferred_element_type=jnp.float32)
        result = result + partial_term.astype(jnp.bfloat16).astype(jnp.float32)
    return result.astype(jnp.bfloat16)
```

```python
import math

import jax
import jax.numpy as jnp
from jax import lax
from jax.sharding import PartitionSpec as P

HD = 128
PAGE_TOK = 64
NEW = 256


masked_fill = -1e30


def shards(
    queries, new_keys, new_values, cache_keys, cache_values, block_table, ancestor_len, out_weight
):
    row_count = queries.shape[0]
    heads_here = queries.shape[1] // HD
    kv_here = new_keys.shape[1] // HD
    group_size = heads_here // kv_here
    slot_count = block_table.shape[1]
    score_scale = 1.0 / math.sqrt(HD)

    q = queries.reshape(row_count, kv_here, group_size, HD).transpose(1, 2, 0, 3)
    own_k = new_keys.reshape(row_count, kv_here, HD).transpose(1, 0, 2)
    own_v = new_values.reshape(row_count, kv_here, HD).transpose(1, 0, 2)

    kv_local = jnp.concatenate([cache_keys, cache_values], axis=-1)
    kv_all = lax.all_gather(kv_local, ("branch", "page"), axis=0, tiled=True)
    kv_sel = jnp.take(kv_all, block_table[0], axis=0)
    anc_len = slot_count * PAGE_TOK
    kv_sel = kv_sel.reshape(anc_len, 2, kv_here, HD)
    anc_k = kv_sel[:, 0].transpose(1, 0, 2)
    anc_v = kv_sel[:, 1].transpose(1, 0, 2)

    own_scores = (
        jnp.einsum("kgnd,kjd->kgnj", q, own_k, preferred_element_type=jnp.float32) * score_scale
    )
    anc_scores = (
        jnp.einsum("kgnd,kjd->kgnj", q, anc_k, preferred_element_type=jnp.float32) * score_scale
    )
    places = jnp.arange(row_count, dtype=jnp.int32)
    own_mask = places[None, :] <= places[:, None]
    anc_mask = jnp.arange(anc_len, dtype=jnp.int32) < ancestor_len[0]
    own_m = jnp.where(own_mask[None, None], own_scores, masked_fill)
    anc_m = jnp.where(anc_mask[None, None, None, :], anc_scores, masked_fill)
    row_max = jnp.maximum(jnp.max(own_m, axis=-1), jnp.max(anc_m, axis=-1))[..., None]
    own_w = jnp.where(own_mask[None, None], jnp.exp(own_scores - row_max), 0.0).astype(jnp.bfloat16)
    anc_w = jnp.where(anc_mask[None, None, None, :], jnp.exp(anc_scores - row_max), 0.0).astype(
        jnp.bfloat16
    )
    denom = jnp.sum(own_w.astype(jnp.float32), axis=-1) + jnp.sum(anc_w.astype(jnp.float32), axis=-1)
    summed = jnp.einsum(
        "kgnj,kjd->kgnd", own_w, own_v, preferred_element_type=jnp.float32
    ) + jnp.einsum("kgnj,kjd->kgnd", anc_w, anc_v, preferred_element_type=jnp.float32)
    attn = (summed / denom[..., None]).astype(jnp.bfloat16)
    attn_out = attn.transpose(2, 0, 1, 3).reshape(row_count, heads_here * HD)

    partial_term = jnp.dot(
        lax.all_gather(attn_out, "page", axis=0, tiled=True),
        out_weight,
        preferred_element_type=jnp.float32,
    ).astype(jnp.bfloat16)
    summed_out = lax.psum_scatter(partial_term, "head", scatter_dimension=0, tiled=True)
    return summed_out


def solution(mesh):
    in_specs = (
        P(("branch", "page"), "head"),
        P(("branch", "page"), "head"),
        P(("branch", "page"), "head"),
        P(("branch", "page"), None, "head"),
        P(("branch", "page"), None, "head"),
        P(("branch", "page"), None),
        P(("branch", "page")),
        P("head", "page"),
    )
    out_specs = P(("branch", "head"), "page")
    return jax.shard_map(shards, mesh=mesh, in_specs=in_specs, out_specs=out_specs, check_vma=False)
```

```python
import math

import jax
import jax.numpy as jnp
import numpy as np
from jax import lax
from jax.sharding import Mesh
from jax.sharding import PartitionSpec as P

HD = 128
PAGE_TOK = 64
NEW = 256


masked_fill = -1e30

PAGE_AXES = ("y", "zl", "core")
ROWS_AXES = ("zl", "core")


def shards(
    queries, new_keys, new_values, cache_keys, cache_values, block_table, ancestor_len, out_weight
):
    row_count = queries.shape[0]
    heads_here = queries.shape[1] // HD
    kv_here = new_keys.shape[1] // HD
    group_size = heads_here // kv_here
    slot_count = block_table.shape[1]
    pages_here = cache_keys.shape[0]
    score_scale = 1.0 / math.sqrt(HD)
    n_head = lax.axis_size("head")
    n_y = lax.axis_size("y")
    n_zl = lax.axis_size("zl")
    n_core = lax.axis_size("core")
    n_chips = lax.axis_size("branch") * n_y * n_zl

    w_group = lax.all_gather(out_weight, "y", axis=1, tiled=True)

    q = queries.reshape(row_count, kv_here, group_size, HD).transpose(1, 2, 0, 3)
    own_k = new_keys.reshape(row_count, kv_here, HD).transpose(1, 0, 2)
    own_v = new_values.reshape(row_count, kv_here, HD).transpose(1, 0, 2)

    kv_local = jnp.concatenate([cache_keys, cache_values], axis=-1)
    kv_chips = lax.all_gather(kv_local, ("branch", "y", "zl"), axis=0, tiled=True)
    kv_all = lax.all_gather(kv_chips, "core", axis=0, tiled=True)
    page = block_table[0]
    owner = page // pages_here
    slot = page % pages_here
    position = ((owner % n_core) * n_chips + owner // n_core) * pages_here + slot
    kv_sel = jnp.take(kv_all, position, axis=0)
    anc_len = slot_count * PAGE_TOK
    kv_sel = kv_sel.reshape(anc_len, 2, kv_here, HD)
    anc_k = kv_sel[:, 0].transpose(1, 0, 2)
    anc_v = kv_sel[:, 1].transpose(1, 0, 2)

    own_scores = (
        jnp.einsum("kgnd,kjd->kgnj", q, own_k, preferred_element_type=jnp.float32) * score_scale
    )
    anc_scores = (
        jnp.einsum("kgnd,kjd->kgnj", q, anc_k, preferred_element_type=jnp.float32) * score_scale
    )
    places = jnp.arange(row_count, dtype=jnp.int32)
    own_mask = places[None, :] <= places[:, None]
    anc_mask = jnp.arange(anc_len, dtype=jnp.int32) < ancestor_len[0]
    own_m = jnp.where(own_mask[None, None], own_scores, masked_fill)
    anc_m = jnp.where(anc_mask[None, None, None, :], anc_scores, masked_fill)
    row_max = jnp.maximum(jnp.max(own_m, axis=-1), jnp.max(anc_m, axis=-1))[..., None]
    own_w = jnp.where(own_mask[None, None], jnp.exp(own_scores - row_max), 0.0).astype(jnp.bfloat16)
    anc_w = jnp.where(anc_mask[None, None, None, :], jnp.exp(anc_scores - row_max), 0.0).astype(
        jnp.bfloat16
    )
    denom = jnp.sum(own_w.astype(jnp.float32), axis=-1) + jnp.sum(anc_w.astype(jnp.float32), axis=-1)
    summed = jnp.einsum(
        "kgnj,kjd->kgnd", own_w, own_v, preferred_element_type=jnp.float32
    ) + jnp.einsum("kgnj,kjd->kgnd", anc_w, anc_v, preferred_element_type=jnp.float32)
    attn = (summed / denom[..., None]).astype(jnp.bfloat16)
    attn_out = attn.transpose(2, 0, 1, 3).reshape(row_count, heads_here * HD)

    attn_rows = lax.all_gather(attn_out, ROWS_AXES, axis=0, tiled=True)
    partial_term = jnp.dot(attn_rows, w_group, preferred_element_type=jnp.float32).astype(
        jnp.bfloat16
    )
    summed_out = lax.psum_scatter(partial_term, "head", scatter_dimension=1, tiled=True)
    swap = [(a * n_y + b, b * n_y + a) for a in range(n_head) for b in range(n_y)]
    return lax.ppermute(summed_out, ("head", "y"), swap)


def solution(mesh):
    n_page = mesh.shape["page"]
    devices = np.asarray(mesh.devices)
    n_core = 2
    n_y = 4
    n_zl = n_page // (n_y * n_core)
    fine = Mesh(
        devices.reshape(mesh.shape["branch"], mesh.shape["head"], n_y, n_zl, n_core),
        ("branch", "head") + PAGE_AXES,
    )
    rows = ("branch",) + PAGE_AXES
    in_specs = (
        P(rows, "head"),
        P(rows, "head"),
        P(rows, "head"),
        P(rows, None, "head"),
        P(rows, None, "head"),
        P(rows, None),
        P(rows),
        P("head", PAGE_AXES),
    )
    out_specs = P(("branch", "head"), PAGE_AXES)
    return jax.shard_map(shards, mesh=fine, in_specs=in_specs, out_specs=out_specs, check_vma=False)
```

```python
import math

import jax
import jax.numpy as jnp
from jax import lax
from jax.sharding import Mesh
from jax.sharding import PartitionSpec as P
import numpy as np

HD = 128
PAGE_TOK = 64
NEW = 256


masked_fill = -1e30


def shards(
    queries, new_keys, new_values, cache_keys, cache_values, block_table, ancestor_len, out_weight
):
    row_count = queries.shape[0]
    heads_here = queries.shape[1] // HD
    kv_here = new_keys.shape[1] // HD
    group_size = heads_here // kv_here
    slot_count = block_table.shape[1]
    score_scale = 1.0 / math.sqrt(HD)

    q = queries.reshape(row_count, kv_here, group_size, HD).transpose(1, 2, 0, 3)
    own_k = new_keys.reshape(row_count, kv_here, HD).transpose(1, 0, 2)
    own_v = new_values.reshape(row_count, kv_here, HD).transpose(1, 0, 2)

    kv_local = jnp.concatenate([cache_keys, cache_values], axis=-1)
    kv_all = lax.all_gather(kv_local, ("branch",) + PAGE_AXES, axis=0, tiled=True)
    kv_sel = jnp.take(kv_all, block_table[0], axis=0)
    anc_len = slot_count * PAGE_TOK
    kv_sel = kv_sel.reshape(anc_len, 2, kv_here, HD)
    anc_k = kv_sel[:, 0].transpose(1, 0, 2)
    anc_v = kv_sel[:, 1].transpose(1, 0, 2)

    own_scores = (
        jnp.einsum("kgnd,kjd->kgnj", q, own_k, preferred_element_type=jnp.float32) * score_scale
    )
    anc_scores = (
        jnp.einsum("kgnd,kjd->kgnj", q, anc_k, preferred_element_type=jnp.float32) * score_scale
    )
    places = jnp.arange(row_count, dtype=jnp.int32)
    own_mask = places[None, :] <= places[:, None]
    anc_mask = jnp.arange(anc_len, dtype=jnp.int32) < ancestor_len[0]
    own_m = jnp.where(own_mask[None, None], own_scores, masked_fill)
    anc_m = jnp.where(anc_mask[None, None, None, :], anc_scores, masked_fill)
    row_max = jnp.maximum(jnp.max(own_m, axis=-1), jnp.max(anc_m, axis=-1))[..., None]
    own_w = jnp.where(own_mask[None, None], jnp.exp(own_scores - row_max), 0.0).astype(jnp.bfloat16)
    anc_w = jnp.where(anc_mask[None, None, None, :], jnp.exp(anc_scores - row_max), 0.0).astype(
        jnp.bfloat16
    )
    denom = jnp.sum(own_w.astype(jnp.float32), axis=-1) + jnp.sum(anc_w.astype(jnp.float32), axis=-1)
    summed = jnp.einsum(
        "kgnj,kjd->kgnd", own_w, own_v, preferred_element_type=jnp.float32
    ) + jnp.einsum("kgnj,kjd->kgnd", anc_w, anc_v, preferred_element_type=jnp.float32)
    attn = (summed / denom[..., None]).astype(jnp.bfloat16)
    attn_out = attn.transpose(2, 0, 1, 3).reshape(row_count, heads_here * HD)

    n_y = lax.axis_size("y")
    n_zl = lax.axis_size("zl")
    n_core = lax.axis_size("core")
    attn_chips = lax.all_gather(attn_out, ("y", "zl"), axis=0, tiled=True)
    attn_all = lax.all_gather(attn_chips, "core", axis=0, tiled=True)
    attn_all = attn_all.reshape(n_core, n_y, n_zl * row_count, attn_all.shape[1])
    partial_term = jnp.einsum(
        "cyrk,kf->ycrf", attn_all, out_weight, preferred_element_type=jnp.float32
    ).astype(jnp.bfloat16)
    cols = partial_term.shape[-1]
    partial_term = partial_term.reshape(-1, cols)
    summed_out = lax.psum_scatter(partial_term, "head", scatter_dimension=0, tiled=True)
    summed_out = summed_out.reshape(n_core, n_zl, row_count, cols).transpose(1, 0, 2, 3)
    return summed_out.reshape(n_zl * n_core * row_count, cols)


PAGE_AXES = ("y", "zl", "core")


def solution(mesh):
    n_page = mesh.shape["page"]
    n_core = 2
    n_y = 4
    fine = Mesh(
        np.asarray(mesh.devices).reshape(
            mesh.shape["branch"], mesh.shape["head"], n_y, n_page // (n_y * n_core), n_core
        ),
        ("branch", "head") + PAGE_AXES,
    )
    rows = ("branch",) + PAGE_AXES
    in_specs = (
        P(rows, "head"),
        P(rows, "head"),
        P(rows, "head"),
        P(rows, None, "head"),
        P(rows, None, "head"),
        P(rows, None),
        P(rows),
        P("head", PAGE_AXES),
    )
    out_specs = P(("branch", "head"), PAGE_AXES)
    return jax.shard_map(shards, mesh=fine, in_specs=in_specs, out_specs=out_specs, check_vma=False)
```

```python
import math

import jax
import jax.numpy as jnp
from jax import lax
from jax.sharding import PartitionSpec as P

HD = 128
PAGE_TOK = 64
NEW = 256


masked_fill = -1e30


def shards(
    queries, new_keys, new_values, cache_keys, cache_values, block_table, ancestor_len, out_weight
):
    row_count = queries.shape[0]
    heads_here = queries.shape[1] // HD
    kv_here = new_keys.shape[1] // HD
    group_size = heads_here // kv_here
    slot_count = block_table.shape[1]
    score_scale = 1.0 / math.sqrt(HD)

    q = queries.reshape(row_count, kv_here, group_size, HD).transpose(1, 2, 0, 3)
    own_k = new_keys.reshape(row_count, kv_here, HD).transpose(1, 0, 2)
    own_v = new_values.reshape(row_count, kv_here, HD).transpose(1, 0, 2)

    kv_local = jnp.concatenate([cache_keys, cache_values], axis=-1)
    kv_all = lax.all_gather(kv_local, ("branch", "page"), axis=0, tiled=True)
    kv_sel = jnp.take(kv_all, block_table[0], axis=0)
    anc_len = slot_count * PAGE_TOK
    kv_sel = kv_sel.reshape(anc_len, 2, kv_here, HD)
    anc_k = kv_sel[:, 0].transpose(1, 0, 2)
    anc_v = kv_sel[:, 1].transpose(1, 0, 2)

    own_scores = (
        jnp.einsum("kgnd,kjd->kgnj", q, own_k, preferred_element_type=jnp.float32) * score_scale
    )
    anc_scores = (
        jnp.einsum("kgnd,kjd->kgnj", q, anc_k, preferred_element_type=jnp.float32) * score_scale
    )
    places = jnp.arange(row_count, dtype=jnp.int32)
    own_mask = places[None, :] <= places[:, None]
    anc_mask = jnp.arange(anc_len, dtype=jnp.int32) < ancestor_len[0]
    own_m = jnp.where(own_mask[None, None], own_scores, masked_fill)
    anc_m = jnp.where(anc_mask[None, None, None, :], anc_scores, masked_fill)
    row_max = jnp.maximum(jnp.max(own_m, axis=-1), jnp.max(anc_m, axis=-1))[..., None]
    own_w = jnp.where(own_mask[None, None], jnp.exp(own_scores - row_max), 0.0).astype(jnp.bfloat16)
    anc_w = jnp.where(anc_mask[None, None, None, :], jnp.exp(anc_scores - row_max), 0.0).astype(
        jnp.bfloat16
    )
    denom = jnp.sum(own_w.astype(jnp.float32), axis=-1) + jnp.sum(anc_w.astype(jnp.float32), axis=-1)
    summed = jnp.einsum(
        "kgnj,kjd->kgnd", own_w, own_v, preferred_element_type=jnp.float32
    ) + jnp.einsum("kgnj,kjd->kgnd", anc_w, anc_v, preferred_element_type=jnp.float32)
    attn = (summed / denom[..., None]).astype(jnp.bfloat16)
    attn_out = attn.transpose(2, 0, 1, 3).reshape(row_count, heads_here * HD)

    n_head = lax.axis_size("head")
    chunk = row_count // CHUNKS
    pieces = []
    for index in range(CHUNKS):
        rows_here = attn_out[index * chunk:(index + 1) * chunk]
        gathered = lax.all_gather(rows_here, "page", axis=0, tiled=True)
        partial_term = jnp.dot(gathered, out_weight, preferred_element_type=jnp.float32).astype(
            jnp.bfloat16
        )
        cols = partial_term.shape[1]
        partial_term = partial_term.reshape(n_head, -1, cols)
        arrived = lax.all_to_all(partial_term, "head", 0, 0, tiled=True)
        pieces.append(jnp.sum(arrived.astype(jnp.float32), axis=0).astype(jnp.bfloat16))
    out = jnp.stack(pieces).reshape(CHUNKS, -1, chunk, pieces[0].shape[-1])
    return out.transpose(1, 0, 2, 3).reshape(-1, out.shape[-1])


CHUNKS = 4


def solution(mesh):
    in_specs = (
        P(("branch", "page"), "head"),
        P(("branch", "page"), "head"),
        P(("branch", "page"), "head"),
        P(("branch", "page"), None, "head"),
        P(("branch", "page"), None, "head"),
        P(("branch", "page"), None),
        P(("branch", "page")),
        P("head", "page"),
    )
    out_specs = P(("branch", "head"), "page")
    return jax.shard_map(shards, mesh=mesh, in_specs=in_specs, out_specs=out_specs, check_vma=False)
```

```python
import math

import jax
import jax.numpy as jnp
from jax import lax
from jax.sharding import PartitionSpec as P

HD = 128
PAGE_TOK = 64
NEW = 256


masked_fill = -1e30


def shards(
    queries, new_keys, new_values, cache_keys, cache_values, block_table, ancestor_len, out_weight
):
    row_count = queries.shape[0]
    heads_here = queries.shape[1] // HD
    kv_here = new_keys.shape[1] // HD
    group_size = heads_here // kv_here
    slot_count = block_table.shape[1]
    score_scale = 1.0 / math.sqrt(HD)

    q = queries.reshape(row_count, kv_here, group_size, HD).transpose(1, 2, 0, 3)
    own_k = new_keys.reshape(row_count, kv_here, HD).transpose(1, 0, 2)
    own_v = new_values.reshape(row_count, kv_here, HD).transpose(1, 0, 2)

    kv_local = jnp.concatenate([cache_keys, cache_values], axis=-1)
    kv_all = gather_by_all_to_all(kv_local, ("branch", "page"))
    kv_sel = jnp.take(kv_all, block_table[0], axis=0)
    anc_len = slot_count * PAGE_TOK
    kv_sel = kv_sel.reshape(anc_len, 2, kv_here, HD)
    anc_k = kv_sel[:, 0].transpose(1, 0, 2)
    anc_v = kv_sel[:, 1].transpose(1, 0, 2)

    own_scores = (
        jnp.einsum("kgnd,kjd->kgnj", q, own_k, preferred_element_type=jnp.float32) * score_scale
    )
    anc_scores = (
        jnp.einsum("kgnd,kjd->kgnj", q, anc_k, preferred_element_type=jnp.float32) * score_scale
    )
    places = jnp.arange(row_count, dtype=jnp.int32)
    own_mask = places[None, :] <= places[:, None]
    anc_mask = jnp.arange(anc_len, dtype=jnp.int32) < ancestor_len[0]
    own_m = jnp.where(own_mask[None, None], own_scores, masked_fill)
    anc_m = jnp.where(anc_mask[None, None, None, :], anc_scores, masked_fill)
    row_max = jnp.maximum(jnp.max(own_m, axis=-1), jnp.max(anc_m, axis=-1))[..., None]
    own_w = jnp.where(own_mask[None, None], jnp.exp(own_scores - row_max), 0.0).astype(jnp.bfloat16)
    anc_w = jnp.where(anc_mask[None, None, None, :], jnp.exp(anc_scores - row_max), 0.0).astype(
        jnp.bfloat16
    )
    denom = jnp.sum(own_w.astype(jnp.float32), axis=-1) + jnp.sum(anc_w.astype(jnp.float32), axis=-1)
    summed = jnp.einsum(
        "kgnj,kjd->kgnd", own_w, own_v, preferred_element_type=jnp.float32
    ) + jnp.einsum("kgnj,kjd->kgnd", anc_w, anc_v, preferred_element_type=jnp.float32)
    attn = (summed / denom[..., None]).astype(jnp.bfloat16)
    attn_out = attn.transpose(2, 0, 1, 3).reshape(row_count, heads_here * HD)

    n_head = lax.axis_size("head")
    partial_term = jnp.dot(
        gather_by_all_to_all(attn_out, "page"), out_weight, preferred_element_type=jnp.float32
    ).astype(jnp.bfloat16)
    cols = partial_term.shape[1]
    arrived = lax.all_to_all(partial_term.reshape(n_head, -1, cols), "head", 0, 0, tiled=True)
    return jnp.sum(arrived.astype(jnp.float32), axis=0).astype(jnp.bfloat16)


def gather_by_all_to_all(x, axes):
    count = lax.axis_size(axes)
    spread = jnp.broadcast_to(x[None], (count,) + x.shape)
    arrived = lax.all_to_all(spread, axes, 0, 0, tiled=True)
    return arrived.reshape((count * x.shape[0],) + x.shape[1:])


def solution(mesh):
    in_specs = (
        P(("branch", "page"), "head"),
        P(("branch", "page"), "head"),
        P(("branch", "page"), "head"),
        P(("branch", "page"), None, "head"),
        P(("branch", "page"), None, "head"),
        P(("branch", "page"), None),
        P(("branch", "page")),
        P("head", "page"),
    )
    out_specs = P(("branch", "head"), "page")
    return jax.shard_map(shards, mesh=mesh, in_specs=in_specs, out_specs=out_specs, check_vma=False)
```

```python
import math

import jax
import jax.numpy as jnp
from jax import lax
from jax.sharding import Mesh
from jax.sharding import PartitionSpec as P
import numpy as np

HD = 128
PAGE_TOK = 64
NEW = 256


masked_fill = -1e30


def shards(
    queries, new_keys, new_values, cache_keys, cache_values, block_table, ancestor_len, out_weight
):
    row_count = queries.shape[0]
    heads_here = queries.shape[1] // HD
    kv_here = new_keys.shape[1] // HD
    group_size = heads_here // kv_here
    slot_count = block_table.shape[1]
    score_scale = 1.0 / math.sqrt(HD)

    w_cols = lax.all_gather(out_weight, ZC, axis=1, tiled=True)

    q = queries.reshape(row_count, kv_here, group_size, HD).transpose(1, 2, 0, 3)
    own_k = new_keys.reshape(row_count, kv_here, HD).transpose(1, 0, 2)
    own_v = new_values.reshape(row_count, kv_here, HD).transpose(1, 0, 2)

    kv_local = jnp.concatenate([cache_keys, cache_values], axis=-1)
    kv_all = gather_by_all_to_all(kv_local, ("branch",) + PAGE_AXES)
    kv_sel = jnp.take(kv_all, block_table[0], axis=0)
    anc_len = slot_count * PAGE_TOK
    kv_sel = kv_sel.reshape(anc_len, 2, kv_here, HD)
    anc_k = kv_sel[:, 0].transpose(1, 0, 2)
    anc_v = kv_sel[:, 1].transpose(1, 0, 2)

    own_scores = (
        jnp.einsum("kgnd,kjd->kgnj", q, own_k, preferred_element_type=jnp.float32) * score_scale
    )
    anc_scores = (
        jnp.einsum("kgnd,kjd->kgnj", q, anc_k, preferred_element_type=jnp.float32) * score_scale
    )
    places = jnp.arange(row_count, dtype=jnp.int32)
    own_mask = places[None, :] <= places[:, None]
    anc_mask = jnp.arange(anc_len, dtype=jnp.int32) < ancestor_len[0]
    own_m = jnp.where(own_mask[None, None], own_scores, masked_fill)
    anc_m = jnp.where(anc_mask[None, None, None, :], anc_scores, masked_fill)
    row_max = jnp.maximum(jnp.max(own_m, axis=-1), jnp.max(anc_m, axis=-1))[..., None]
    own_w = jnp.where(own_mask[None, None], jnp.exp(own_scores - row_max), 0.0).astype(jnp.bfloat16)
    anc_w = jnp.where(anc_mask[None, None, None, :], jnp.exp(anc_scores - row_max), 0.0).astype(
        jnp.bfloat16
    )
    denom = jnp.sum(own_w.astype(jnp.float32), axis=-1) + jnp.sum(anc_w.astype(jnp.float32), axis=-1)
    summed = jnp.einsum(
        "kgnj,kjd->kgnd", own_w, own_v, preferred_element_type=jnp.float32
    ) + jnp.einsum("kgnj,kjd->kgnd", anc_w, anc_v, preferred_element_type=jnp.float32)
    attn = (summed / denom[..., None]).astype(jnp.bfloat16)
    attn_out = attn.transpose(2, 0, 1, 3).reshape(row_count, heads_here * HD)

    attn_rows = lax.all_gather(attn_out, "y", axis=0, tiled=True)
    partial_term = jnp.dot(attn_rows, w_cols, preferred_element_type=jnp.float32).astype(
        jnp.bfloat16
    )
    summed = lax.psum_scatter(partial_term, "head", scatter_dimension=0, tiled=True)
    n_zc = lax.axis_size(ZC)
    cols = out_weight.shape[1]
    summed = summed.reshape(row_count, n_zc, cols).transpose(1, 0, 2)
    arrived = lax.all_to_all(summed, ZC, 0, 0, tiled=True)
    return arrived.reshape(n_zc * row_count, cols)


def gather_by_all_to_all(x, axes):
    count = lax.axis_size(axes)
    spread = jnp.broadcast_to(x[None], (count,) + x.shape)
    arrived = lax.all_to_all(spread, axes, 0, 0, tiled=True)
    return arrived.reshape((count * x.shape[0],) + x.shape[1:])


PAGE_AXES = ("y", "zl", "core")
ZC = ("zl", "core")


def solution(mesh):
    n_page = mesh.shape["page"]
    n_core = 2
    n_y = 4
    fine = Mesh(
        np.asarray(mesh.devices).reshape(
            mesh.shape["branch"], mesh.shape["head"], n_y, n_page // (n_y * n_core), n_core
        ),
        ("branch", "head") + PAGE_AXES,
    )
    rows = ("branch",) + PAGE_AXES
    in_specs = (
        P(rows, "head"),
        P(rows, "head"),
        P(rows, "head"),
        P(rows, None, "head"),
        P(rows, None, "head"),
        P(rows, None),
        P(rows),
        P("head", PAGE_AXES),
    )
    out_specs = P(("branch", "head"), PAGE_AXES)
    return jax.shard_map(shards, mesh=fine, in_specs=in_specs, out_specs=out_specs, check_vma=False)
```

```python
import math

import jax
import jax.numpy as jnp
from jax import lax
from jax.sharding import Mesh
from jax.sharding import PartitionSpec as P
import numpy as np

HD = 128
PAGE_TOK = 64
NEW = 256


masked_fill = -1e30


def shards(
    queries, new_keys, new_values, cache_keys, cache_values, block_table, ancestor_len, out_weight
):
    row_count = queries.shape[0]
    heads_here = queries.shape[1] // HD
    kv_here = new_keys.shape[1] // HD
    group_size = heads_here // kv_here
    slot_count = block_table.shape[1]
    score_scale = 1.0 / math.sqrt(HD)

    w_cols = lax.all_gather(out_weight, ZC, axis=1, tiled=True)

    q = queries.reshape(row_count, kv_here, group_size, HD).transpose(1, 2, 0, 3)
    own_k = new_keys.reshape(row_count, kv_here, HD).transpose(1, 0, 2)
    own_v = new_values.reshape(row_count, kv_here, HD).transpose(1, 0, 2)

    kv_local = jnp.concatenate([cache_keys, cache_values], axis=-1)
    kv_all = gather_by_all_to_all(kv_local, ("branch",) + PAGE_AXES)
    kv_sel = jnp.take(kv_all, block_table[0], axis=0)
    anc_len = slot_count * PAGE_TOK
    kv_sel = kv_sel.reshape(anc_len, 2, kv_here, HD)
    anc_k = kv_sel[:, 0].transpose(1, 0, 2)
    anc_v = kv_sel[:, 1].transpose(1, 0, 2)

    own_scores = (
        jnp.einsum("kgnd,kjd->kgnj", q, own_k, preferred_element_type=jnp.float32) * score_scale
    )
    anc_scores = (
        jnp.einsum("kgnd,kjd->kgnj", q, anc_k, preferred_element_type=jnp.float32) * score_scale
    )
    places = jnp.arange(row_count, dtype=jnp.int32)
    own_mask = places[None, :] <= places[:, None]
    anc_mask = jnp.arange(anc_len, dtype=jnp.int32) < ancestor_len[0]
    own_m = jnp.where(own_mask[None, None], own_scores, masked_fill)
    anc_m = jnp.where(anc_mask[None, None, None, :], anc_scores, masked_fill)
    row_max = jnp.maximum(jnp.max(own_m, axis=-1), jnp.max(anc_m, axis=-1))[..., None]
    own_w = jnp.where(own_mask[None, None], jnp.exp(own_scores - row_max), 0.0).astype(jnp.bfloat16)
    anc_w = jnp.where(anc_mask[None, None, None, :], jnp.exp(anc_scores - row_max), 0.0).astype(
        jnp.bfloat16
    )
    denom = jnp.sum(own_w.astype(jnp.float32), axis=-1) + jnp.sum(anc_w.astype(jnp.float32), axis=-1)
    summed = jnp.einsum(
        "kgnj,kjd->kgnd", own_w, own_v, preferred_element_type=jnp.float32
    ) + jnp.einsum("kgnj,kjd->kgnd", anc_w, anc_v, preferred_element_type=jnp.float32)
    attn = (summed / denom[..., None]).astype(jnp.bfloat16)
    attn_out = attn.transpose(2, 0, 1, 3).reshape(row_count, heads_here * HD)

    attn_rows = gather_by_all_to_all(attn_out, "y")
    partial_term = jnp.dot(attn_rows, w_cols, preferred_element_type=jnp.float32).astype(
        jnp.bfloat16
    )
    summed = lax.psum_scatter(partial_term, "head", scatter_dimension=0, tiled=True)
    n_zc = lax.axis_size(ZC)
    cols = out_weight.shape[1]
    summed = summed.reshape(row_count, n_zc, cols).transpose(1, 0, 2)
    arrived = lax.all_to_all(summed, ZC, 0, 0, tiled=True)
    return arrived.reshape(n_zc * row_count, cols)


def gather_by_all_to_all(x, axes):
    count = lax.axis_size(axes)
    spread = jnp.broadcast_to(x[None], (count,) + x.shape)
    arrived = lax.all_to_all(spread, axes, 0, 0, tiled=True)
    return arrived.reshape((count * x.shape[0],) + x.shape[1:])


PAGE_AXES = ("y", "zl", "core")
ZC = ("zl", "core")


def solution(mesh):
    n_page = mesh.shape["page"]
    n_core = 2
    n_y = 4
    fine = Mesh(
        np.asarray(mesh.devices).reshape(
            mesh.shape["branch"], mesh.shape["head"], n_y, n_page // (n_y * n_core), n_core
        ),
        ("branch", "head") + PAGE_AXES,
    )
    rows = ("branch",) + PAGE_AXES
    in_specs = (
        P(rows, "head"),
        P(rows, "head"),
        P(rows, "head"),
        P(rows, None, "head"),
        P(rows, None, "head"),
        P(rows, None),
        P(rows),
        P("head", PAGE_AXES),
    )
    out_specs = P(("branch", "head"), PAGE_AXES)
    return jax.shard_map(shards, mesh=fine, in_specs=in_specs, out_specs=out_specs, check_vma=False)
```

```python
import math

import jax
import jax.numpy as jnp
from jax import lax
from jax.sharding import Mesh
from jax.sharding import PartitionSpec as P
import numpy as np

HD = 128
PAGE_TOK = 64
NEW = 256


masked_fill = -1e30


def shards(
    queries, new_keys, new_values, cache_keys, cache_values, block_table, ancestor_len, out_weight
):
    row_count = queries.shape[0]
    heads_here = queries.shape[1] // HD
    kv_here = new_keys.shape[1] // HD
    group_size = heads_here // kv_here
    slot_count = block_table.shape[1]
    score_scale = 1.0 / math.sqrt(HD)

    w_stack = gather_by_all_to_all(out_weight[None], ZC)

    q = queries.reshape(row_count, kv_here, group_size, HD).transpose(1, 2, 0, 3)
    own_k = new_keys.reshape(row_count, kv_here, HD).transpose(1, 0, 2)
    own_v = new_values.reshape(row_count, kv_here, HD).transpose(1, 0, 2)

    kv_local = jnp.concatenate([cache_keys, cache_values], axis=-1)
    kv_all = lax.all_gather(kv_local, ("branch",) + PAGE_AXES, axis=0, tiled=True)
    kv_sel = jnp.take(kv_all, block_table[0], axis=0)
    anc_len = slot_count * PAGE_TOK
    kv_sel = kv_sel.reshape(anc_len, 2, kv_here, HD)
    anc_k = kv_sel[:, 0].transpose(1, 0, 2)
    anc_v = kv_sel[:, 1].transpose(1, 0, 2)

    own_scores = (
        jnp.einsum("kgnd,kjd->kgnj", q, own_k, preferred_element_type=jnp.float32) * score_scale
    )
    anc_scores = (
        jnp.einsum("kgnd,kjd->kgnj", q, anc_k, preferred_element_type=jnp.float32) * score_scale
    )
    places = jnp.arange(row_count, dtype=jnp.int32)
    own_mask = places[None, :] <= places[:, None]
    anc_mask = jnp.arange(anc_len, dtype=jnp.int32) < ancestor_len[0]
    own_m = jnp.where(own_mask[None, None], own_scores, masked_fill)
    anc_m = jnp.where(anc_mask[None, None, None, :], anc_scores, masked_fill)
    row_max = jnp.maximum(jnp.max(own_m, axis=-1), jnp.max(anc_m, axis=-1))[..., None]
    own_w = jnp.where(own_mask[None, None], jnp.exp(own_scores - row_max), 0.0).astype(jnp.bfloat16)
    anc_w = jnp.where(anc_mask[None, None, None, :], jnp.exp(anc_scores - row_max), 0.0).astype(
        jnp.bfloat16
    )
    denom = jnp.sum(own_w.astype(jnp.float32), axis=-1) + jnp.sum(anc_w.astype(jnp.float32), axis=-1)
    summed = jnp.einsum(
        "kgnj,kjd->kgnd", own_w, own_v, preferred_element_type=jnp.float32
    ) + jnp.einsum("kgnj,kjd->kgnd", anc_w, anc_v, preferred_element_type=jnp.float32)
    attn = (summed / denom[..., None]).astype(jnp.bfloat16)
    attn_out = attn.transpose(2, 0, 1, 3).reshape(row_count, heads_here * HD)

    attn_rows = gather_by_all_to_all(attn_out, "y")
    partial_term = jnp.einsum(
        "rk,jkc->rjc", attn_rows, w_stack, preferred_element_type=jnp.float32
    ).astype(jnp.bfloat16)
    partial_term = partial_term.reshape(partial_term.shape[0], -1)
    summed = lax.psum_scatter(partial_term, "head", scatter_dimension=0, tiled=True)
    n_zc = lax.axis_size(ZC)
    cols = out_weight.shape[1]
    summed = summed.reshape(row_count, n_zc, cols).transpose(1, 0, 2)
    arrived = lax.all_to_all(summed, ZC, 0, 0, tiled=True)
    return arrived.reshape(n_zc * row_count, cols)


def gather_by_all_to_all(x, axes):
    count = lax.axis_size(axes)
    spread = jnp.broadcast_to(x[None], (count,) + x.shape)
    arrived = lax.all_to_all(spread, axes, 0, 0, tiled=True)
    return arrived.reshape((count * x.shape[0],) + x.shape[1:])


PAGE_AXES = ("y", "zl", "core")
ZC = ("zl", "core")


def solution(mesh):
    n_page = mesh.shape["page"]
    n_core = 2
    n_y = 4
    fine = Mesh(
        np.asarray(mesh.devices).reshape(
            mesh.shape["branch"], mesh.shape["head"], n_y, n_page // (n_y * n_core), n_core
        ),
        ("branch", "head") + PAGE_AXES,
    )
    rows = ("branch",) + PAGE_AXES
    in_specs = (
        P(rows, "head"),
        P(rows, "head"),
        P(rows, "head"),
        P(rows, None, "head"),
        P(rows, None, "head"),
        P(rows, None),
        P(rows),
        P("head", PAGE_AXES),
    )
    out_specs = P(("branch", "head"), PAGE_AXES)
    return jax.shard_map(shards, mesh=fine, in_specs=in_specs, out_specs=out_specs, check_vma=False)
```

```python
import math

import jax
import jax.numpy as jnp
from jax import lax
from jax.sharding import Mesh
from jax.sharding import PartitionSpec as P
import numpy as np

HD = 128
PAGE_TOK = 64
NEW = 256


masked_fill = -1e30


def shards(
    queries, new_keys, new_values, cache_keys, cache_values, block_table, ancestor_len, out_weight
):
    row_count = queries.shape[0]
    heads_here = queries.shape[1] // HD
    kv_here = new_keys.shape[1] // HD
    group_size = heads_here // kv_here
    slot_count = block_table.shape[1]
    score_scale = 1.0 / math.sqrt(HD)

    q = queries.reshape(row_count, kv_here, group_size, HD).transpose(1, 2, 0, 3)
    own_k = new_keys.reshape(row_count, kv_here, HD).transpose(1, 0, 2)
    own_v = new_values.reshape(row_count, kv_here, HD).transpose(1, 0, 2)

    kv_local = jnp.concatenate([cache_keys, cache_values], axis=-1)
    kv_all = gather_by_all_to_all(kv_local, ("branch",) + PAGE_AXES)
    out_weight, kv_all = lax.optimization_barrier((out_weight, kv_all))
    w_cols = lax.all_gather(out_weight, ZC, axis=1, tiled=True)
    kv_sel = jnp.take(kv_all, block_table[0], axis=0)
    anc_len = slot_count * PAGE_TOK
    kv_sel = kv_sel.reshape(anc_len, 2, kv_here, HD)
    anc_k = kv_sel[:, 0].transpose(1, 0, 2)
    anc_v = kv_sel[:, 1].transpose(1, 0, 2)

    own_scores = (
        jnp.einsum("kgnd,kjd->kgnj", q, own_k, preferred_element_type=jnp.float32) * score_scale
    )
    anc_scores = (
        jnp.einsum("kgnd,kjd->kgnj", q, anc_k, preferred_element_type=jnp.float32) * score_scale
    )
    places = jnp.arange(row_count, dtype=jnp.int32)
    own_mask = places[None, :] <= places[:, None]
    anc_mask = jnp.arange(anc_len, dtype=jnp.int32) < ancestor_len[0]
    own_m = jnp.where(own_mask[None, None], own_scores, masked_fill)
    anc_m = jnp.where(anc_mask[None, None, None, :], anc_scores, masked_fill)
    row_max = jnp.maximum(jnp.max(own_m, axis=-1), jnp.max(anc_m, axis=-1))[..., None]
    own_w = jnp.where(own_mask[None, None], jnp.exp(own_scores - row_max), 0.0).astype(jnp.bfloat16)
    anc_w = jnp.where(anc_mask[None, None, None, :], jnp.exp(anc_scores - row_max), 0.0).astype(
        jnp.bfloat16
    )
    denom = jnp.sum(own_w.astype(jnp.float32), axis=-1) + jnp.sum(anc_w.astype(jnp.float32), axis=-1)
    summed = jnp.einsum(
        "kgnj,kjd->kgnd", own_w, own_v, preferred_element_type=jnp.float32
    ) + jnp.einsum("kgnj,kjd->kgnd", anc_w, anc_v, preferred_element_type=jnp.float32)
    attn = (summed / denom[..., None]).astype(jnp.bfloat16)
    attn_out = attn.transpose(2, 0, 1, 3).reshape(row_count, heads_here * HD)

    attn_rows = gather_by_all_to_all(attn_out, "y")
    partial_term = jnp.dot(attn_rows, w_cols, preferred_element_type=jnp.float32).astype(
        jnp.bfloat16
    )
    summed = lax.psum_scatter(partial_term, "head", scatter_dimension=0, tiled=True)
    n_zc = lax.axis_size(ZC)
    cols = out_weight.shape[1]
    summed = summed.reshape(row_count, n_zc, cols).transpose(1, 0, 2)
    arrived = lax.all_to_all(summed, ZC, 0, 0, tiled=True)
    return arrived.reshape(n_zc * row_count, cols)


def gather_by_all_to_all(x, axes):
    count = lax.axis_size(axes)
    spread = jnp.broadcast_to(x[None], (count,) + x.shape)
    arrived = lax.all_to_all(spread, axes, 0, 0, tiled=True)
    return arrived.reshape((count * x.shape[0],) + x.shape[1:])


PAGE_AXES = ("y", "zl", "core")
ZC = ("zl", "core")


def solution(mesh):
    n_page = mesh.shape["page"]
    n_core = 2
    n_y = 4
    fine = Mesh(
        np.asarray(mesh.devices).reshape(
            mesh.shape["branch"], mesh.shape["head"], n_y, n_page // (n_y * n_core), n_core
        ),
        ("branch", "head") + PAGE_AXES,
    )
    rows = ("branch",) + PAGE_AXES
    in_specs = (
        P(rows, "head"),
        P(rows, "head"),
        P(rows, "head"),
        P(rows, None, "head"),
        P(rows, None, "head"),
        P(rows, None),
        P(rows),
        P("head", PAGE_AXES),
    )
    out_specs = P(("branch", "head"), PAGE_AXES)
    return jax.shard_map(shards, mesh=fine, in_specs=in_specs, out_specs=out_specs, check_vma=False)
```

```python
import math

import jax
import jax.numpy as jnp
from jax import lax
from jax.sharding import Mesh
from jax.sharding import PartitionSpec as P
import numpy as np

HD = 128
PAGE_TOK = 64
NEW = 256


masked_fill = -1e30


def shards(
    queries, new_keys, new_values, cache_keys, cache_values, block_table, ancestor_len, out_weight
):
    row_count = queries.shape[0]
    heads_here = queries.shape[1] // HD
    kv_here = new_keys.shape[1] // HD
    group_size = heads_here // kv_here
    slot_count = block_table.shape[1]
    score_scale = 1.0 / math.sqrt(HD)

    q = queries.reshape(row_count, kv_here, group_size, HD).transpose(1, 2, 0, 3)
    own_k = new_keys.reshape(row_count, kv_here, HD).transpose(1, 0, 2)
    own_v = new_values.reshape(row_count, kv_here, HD).transpose(1, 0, 2)

    kv_local = jnp.concatenate([cache_keys, cache_values], axis=-1)
    kv_chips = gather_by_all_to_all(kv_local, ("branch", "y", "zl"))
    kv_all = gather_by_all_to_all(kv_chips, "core")
    out_weight, kv_all = lax.optimization_barrier((out_weight, kv_all))
    w_cols = lax.all_gather(out_weight, ZC, axis=1, tiled=True)
    pages_here = cache_keys.shape[0]
    n_core = lax.axis_size("core")
    n_chips = lax.axis_size(("branch", "y", "zl"))
    owner = block_table[0] // pages_here
    position = ((owner % n_core) * n_chips + owner // n_core) * pages_here + block_table[0] % pages_here
    kv_sel = jnp.take(kv_all, position, axis=0)
    anc_len = slot_count * PAGE_TOK
    kv_sel = kv_sel.reshape(anc_len, 2, kv_here, HD)
    anc_k = kv_sel[:, 0].transpose(1, 0, 2)
    anc_v = kv_sel[:, 1].transpose(1, 0, 2)

    own_scores = (
        jnp.einsum("kgnd,kjd->kgnj", q, own_k, preferred_element_type=jnp.float32) * score_scale
    )
    anc_scores = (
        jnp.einsum("kgnd,kjd->kgnj", q, anc_k, preferred_element_type=jnp.float32) * score_scale
    )
    places = jnp.arange(row_count, dtype=jnp.int32)
    own_mask = places[None, :] <= places[:, None]
    anc_mask = jnp.arange(anc_len, dtype=jnp.int32) < ancestor_len[0]
    own_m = jnp.where(own_mask[None, None], own_scores, masked_fill)
    anc_m = jnp.where(anc_mask[None, None, None, :], anc_scores, masked_fill)
    row_max = jnp.maximum(jnp.max(own_m, axis=-1), jnp.max(anc_m, axis=-1))[..., None]
    own_w = jnp.where(own_mask[None, None], jnp.exp(own_scores - row_max), 0.0).astype(jnp.bfloat16)
    anc_w = jnp.where(anc_mask[None, None, None, :], jnp.exp(anc_scores - row_max), 0.0).astype(
        jnp.bfloat16
    )
    denom = jnp.sum(own_w.astype(jnp.float32), axis=-1) + jnp.sum(anc_w.astype(jnp.float32), axis=-1)
    summed = jnp.einsum(
        "kgnj,kjd->kgnd", own_w, own_v, preferred_element_type=jnp.float32
    ) + jnp.einsum("kgnj,kjd->kgnd", anc_w, anc_v, preferred_element_type=jnp.float32)
    attn = (summed / denom[..., None]).astype(jnp.bfloat16)
    attn_out = attn.transpose(2, 0, 1, 3).reshape(row_count, heads_here * HD)

    attn_rows = gather_by_all_to_all(attn_out, "y")
    partial_term = jnp.dot(attn_rows, w_cols, preferred_element_type=jnp.float32).astype(
        jnp.bfloat16
    )
    summed = lax.psum_scatter(partial_term, "head", scatter_dimension=0, tiled=True)
    n_zc = lax.axis_size(ZC)
    cols = out_weight.shape[1]
    summed = summed.reshape(row_count, n_zc, cols).transpose(1, 0, 2)
    arrived = lax.all_to_all(summed, ZC, 0, 0, tiled=True)
    return arrived.reshape(n_zc * row_count, cols)


def gather_by_all_to_all(x, axes):
    count = lax.axis_size(axes)
    spread = jnp.broadcast_to(x[None], (count,) + x.shape)
    arrived = lax.all_to_all(spread, axes, 0, 0, tiled=True)
    return arrived.reshape((count * x.shape[0],) + x.shape[1:])


PAGE_AXES = ("y", "zl", "core")
ZC = ("zl", "core")


def solution(mesh):
    n_page = mesh.shape["page"]
    n_core = 2
    n_y = 4
    fine = Mesh(
        np.asarray(mesh.devices).reshape(
            mesh.shape["branch"], mesh.shape["head"], n_y, n_page // (n_y * n_core), n_core
        ),
        ("branch", "head") + PAGE_AXES,
    )
    rows = ("branch",) + PAGE_AXES
    in_specs = (
        P(rows, "head"),
        P(rows, "head"),
        P(rows, "head"),
        P(rows, None, "head"),
        P(rows, None, "head"),
        P(rows, None),
        P(rows),
        P("head", PAGE_AXES),
    )
    out_specs = P(("branch", "head"), PAGE_AXES)
    return jax.shard_map(shards, mesh=fine, in_specs=in_specs, out_specs=out_specs, check_vma=False)
```

```python
import math

import jax
import jax.numpy as jnp
from jax import lax
from jax.sharding import Mesh
from jax.sharding import PartitionSpec as P
import numpy as np

HD = 128
PAGE_TOK = 64
NEW = 256


masked_fill = -1e30


def shards(
    queries, new_keys, new_values, cache_keys, cache_values, block_table, ancestor_len, out_weight
):
    row_count = queries.shape[0]
    heads_here = queries.shape[1] // HD
    kv_here = new_keys.shape[1] // HD
    group_size = heads_here // kv_here
    slot_count = block_table.shape[1]
    score_scale = 1.0 / math.sqrt(HD)

    q = queries.reshape(row_count, kv_here, group_size, HD).transpose(1, 2, 0, 3)
    own_k = new_keys.reshape(row_count, kv_here, HD).transpose(1, 0, 2)
    own_v = new_values.reshape(row_count, kv_here, HD).transpose(1, 0, 2)

    kv_local = jnp.concatenate([cache_keys, cache_values], axis=-1)
    kv_chips = gather_by_all_to_all(kv_local, ("branch", "y", "zl"))
    kv_all = gather_by_all_to_all(kv_chips, "core")
    out_weight, kv_all = lax.optimization_barrier((out_weight, kv_all))
    w_cols = lax.all_gather(out_weight, ZC, axis=1, tiled=True)
    pages_here = cache_keys.shape[0]
    n_core = lax.axis_size("core")
    n_chips = lax.axis_size(("branch", "y", "zl"))
    owner = block_table[0] // pages_here
    position = ((owner % n_core) * n_chips + owner // n_core) * pages_here + block_table[0] % pages_here
    kv_sel = jnp.take(kv_all, position, axis=0)
    anc_len = slot_count * PAGE_TOK
    kv_sel = kv_sel.reshape(anc_len, 2, kv_here, HD)
    anc_k = kv_sel[:, 0].transpose(1, 0, 2)
    anc_v = kv_sel[:, 1].transpose(1, 0, 2)

    own_scores = (
        jnp.einsum("kgnd,kjd->kgnj", q, own_k, preferred_element_type=jnp.float32) * score_scale
    )
    anc_scores = (
        jnp.einsum("kgnd,kjd->kgnj", q, anc_k, preferred_element_type=jnp.float32) * score_scale
    )
    places = jnp.arange(row_count, dtype=jnp.int32)
    own_mask = places[None, :] <= places[:, None]
    anc_mask = jnp.arange(anc_len, dtype=jnp.int32) < ancestor_len[0]
    own_m = jnp.where(own_mask[None, None], own_scores, masked_fill)
    anc_m = jnp.where(anc_mask[None, None, None, :], anc_scores, masked_fill)
    row_max = jnp.maximum(jnp.max(own_m, axis=-1), jnp.max(anc_m, axis=-1))[..., None]
    own_w = jnp.where(own_mask[None, None], jnp.exp(own_scores - row_max), 0.0).astype(jnp.bfloat16)
    anc_w = jnp.where(anc_mask[None, None, None, :], jnp.exp(anc_scores - row_max), 0.0).astype(
        jnp.bfloat16
    )
    denom = jnp.sum(own_w.astype(jnp.float32), axis=-1) + jnp.sum(anc_w.astype(jnp.float32), axis=-1)
    summed = jnp.einsum(
        "kgnj,kjd->kgnd", own_w, own_v, preferred_element_type=jnp.float32
    ) + jnp.einsum("kgnj,kjd->kgnd", anc_w, anc_v, preferred_element_type=jnp.float32)
    attn = (summed / denom[..., None]).astype(jnp.bfloat16)
    attn_out = attn.transpose(2, 0, 1, 3).reshape(row_count, heads_here * HD)

    attn_rows = gather_by_all_to_all(attn_out, "y")
    partial_term = jnp.dot(attn_rows, w_cols, preferred_element_type=jnp.float32).astype(
        jnp.bfloat16
    )
    n_head = lax.axis_size("head")
    half = partial_term.shape[1] // 2
    by_scatter = lax.psum_scatter(partial_term[:, :half], "head", scatter_dimension=0, tiled=True)
    arrived = lax.all_to_all(
        partial_term[:, half:].reshape(n_head, -1, half), "head", 0, 0, tiled=True
    )
    by_exchange = jnp.sum(arrived.astype(jnp.float32), axis=0).astype(jnp.bfloat16)
    summed = jnp.concatenate([by_scatter, by_exchange], axis=1)
    n_zc = lax.axis_size(ZC)
    cols = out_weight.shape[1]
    summed = summed.reshape(row_count, n_zc, cols).transpose(1, 0, 2)
    arrived = lax.all_to_all(summed, ZC, 0, 0, tiled=True)
    return arrived.reshape(n_zc * row_count, cols)


def gather_by_all_to_all(x, axes):
    count = lax.axis_size(axes)
    spread = jnp.broadcast_to(x[None], (count,) + x.shape)
    arrived = lax.all_to_all(spread, axes, 0, 0, tiled=True)
    return arrived.reshape((count * x.shape[0],) + x.shape[1:])


PAGE_AXES = ("y", "zl", "core")
ZC = ("zl", "core")


def solution(mesh):
    n_page = mesh.shape["page"]
    n_core = 2
    n_y = 4
    fine = Mesh(
        np.asarray(mesh.devices).reshape(
            mesh.shape["branch"], mesh.shape["head"], n_y, n_page // (n_y * n_core), n_core
        ),
        ("branch", "head") + PAGE_AXES,
    )
    rows = ("branch",) + PAGE_AXES
    in_specs = (
        P(rows, "head"),
        P(rows, "head"),
        P(rows, "head"),
        P(rows, None, "head"),
        P(rows, None, "head"),
        P(rows, None),
        P(rows),
        P("head", PAGE_AXES),
    )
    out_specs = P(("branch", "head"), PAGE_AXES)
    return jax.shard_map(shards, mesh=fine, in_specs=in_specs, out_specs=out_specs, check_vma=False)
```

```python
import math

import jax
import jax.numpy as jnp
from jax import lax
from jax.sharding import Mesh
from jax.sharding import PartitionSpec as P
import numpy as np

HD = 128
PAGE_TOK = 64
NEW = 256


masked_fill = -1e30


def shards(
    queries, new_keys, new_values, cache_keys, cache_values, block_table, ancestor_len, out_weight
):
    row_count = queries.shape[0]
    heads_here = queries.shape[1] // HD
    kv_here = new_keys.shape[1] // HD
    group_size = heads_here // kv_here
    slot_count = block_table.shape[1]
    score_scale = 1.0 / math.sqrt(HD)

    q = queries.reshape(row_count, kv_here, group_size, HD).transpose(1, 2, 0, 3)
    own_k = new_keys.reshape(row_count, kv_here, HD).transpose(1, 0, 2)
    own_v = new_values.reshape(row_count, kv_here, HD).transpose(1, 0, 2)

    kv_local = jnp.concatenate([cache_keys, cache_values], axis=-1)
    kv_chips = gather_by_all_to_all(kv_local, ("branch", "y", "zl"))
    kv_all = gather_by_all_to_all(kv_chips, "core")
    out_weight, kv_all = lax.optimization_barrier((out_weight, kv_all))
    w_cols = lax.all_gather(out_weight, ZC, axis=1, tiled=True)
    pages_here = cache_keys.shape[0]
    n_core = lax.axis_size("core")
    n_chips = lax.axis_size(("branch", "y", "zl"))
    owner = block_table[0] // pages_here
    position = ((owner % n_core) * n_chips + owner // n_core) * pages_here + block_table[0] % pages_here
    kv_sel = jnp.take(kv_all, position, axis=0)
    anc_len = slot_count * PAGE_TOK
    kv_sel = kv_sel.reshape(anc_len, 2, kv_here, HD)
    anc_k = kv_sel[:, 0].transpose(1, 0, 2)
    anc_v = kv_sel[:, 1].transpose(1, 0, 2)

    places = jnp.arange(row_count, dtype=jnp.int32)
    own_mask = places[None, :] <= places[:, None]
    anc_mask = jnp.arange(anc_len, dtype=jnp.int32) < ancestor_len[0]
    split = group_size // 2
    partial_f32 = None
    for lower in (0, split):
        q_half = q[:, lower:lower + split]
        attn_half = attend(q_half, own_k, own_v, anc_k, anc_v, own_mask, anc_mask, score_scale)
        attn_half = attn_half.transpose(2, 0, 1, 3).reshape(row_count, kv_here * split * HD)
        rows_half = gather_by_all_to_all(attn_half, "y")
        w_half = w_cols.reshape(kv_here, group_size, HD, -1)[:, lower:lower + split]
        term = jnp.dot(
            rows_half, w_half.reshape(kv_here * split * HD, -1), preferred_element_type=jnp.float32
        )
        partial_f32 = term if partial_f32 is None else partial_f32 + term
    partial_term = partial_f32.astype(jnp.bfloat16)
    summed = lax.psum_scatter(partial_term, "head", scatter_dimension=0, tiled=True)
    n_zc = lax.axis_size(ZC)
    cols = out_weight.shape[1]
    summed = summed.reshape(row_count, n_zc, cols).transpose(1, 0, 2)
    arrived = lax.all_to_all(summed, ZC, 0, 0, tiled=True)
    return arrived.reshape(n_zc * row_count, cols)


def attend(q, own_k, own_v, anc_k, anc_v, own_mask, anc_mask, score_scale):
    own_scores = (
        jnp.einsum("kgnd,kjd->kgnj", q, own_k, preferred_element_type=jnp.float32) * score_scale
    )
    anc_scores = (
        jnp.einsum("kgnd,kjd->kgnj", q, anc_k, preferred_element_type=jnp.float32) * score_scale
    )
    own_m = jnp.where(own_mask[None, None], own_scores, masked_fill)
    anc_m = jnp.where(anc_mask[None, None, None, :], anc_scores, masked_fill)
    row_max = jnp.maximum(jnp.max(own_m, axis=-1), jnp.max(anc_m, axis=-1))[..., None]
    own_w = jnp.where(own_mask[None, None], jnp.exp(own_scores - row_max), 0.0).astype(jnp.bfloat16)
    anc_w = jnp.where(anc_mask[None, None, None, :], jnp.exp(anc_scores - row_max), 0.0).astype(
        jnp.bfloat16
    )
    denom = jnp.sum(own_w.astype(jnp.float32), axis=-1) + jnp.sum(anc_w.astype(jnp.float32), axis=-1)
    summed = jnp.einsum(
        "kgnj,kjd->kgnd", own_w, own_v, preferred_element_type=jnp.float32
    ) + jnp.einsum("kgnj,kjd->kgnd", anc_w, anc_v, preferred_element_type=jnp.float32)
    return (summed / denom[..., None]).astype(jnp.bfloat16)


def gather_by_all_to_all(x, axes):
    count = lax.axis_size(axes)
    spread = jnp.broadcast_to(x[None], (count,) + x.shape)
    arrived = lax.all_to_all(spread, axes, 0, 0, tiled=True)
    return arrived.reshape((count * x.shape[0],) + x.shape[1:])


PAGE_AXES = ("y", "zl", "core")
ZC = ("zl", "core")


def solution(mesh):
    n_page = mesh.shape["page"]
    n_core = 2
    n_y = 4
    fine = Mesh(
        np.asarray(mesh.devices).reshape(
            mesh.shape["branch"], mesh.shape["head"], n_y, n_page // (n_y * n_core), n_core
        ),
        ("branch", "head") + PAGE_AXES,
    )
    rows = ("branch",) + PAGE_AXES
    in_specs = (
        P(rows, "head"),
        P(rows, "head"),
        P(rows, "head"),
        P(rows, None, "head"),
        P(rows, None, "head"),
        P(rows, None),
        P(rows),
        P("head", PAGE_AXES),
    )
    out_specs = P(("branch", "head"), PAGE_AXES)
    return jax.shard_map(shards, mesh=fine, in_specs=in_specs, out_specs=out_specs, check_vma=False)
```

```python
import math

import jax
import jax.numpy as jnp
from jax import lax
from jax.sharding import Mesh
from jax.sharding import PartitionSpec as P
import numpy as np

HD = 128
PAGE_TOK = 64
NEW = 256


masked_fill = -1e30


def shards(
    queries, new_keys, new_values, cache_keys, cache_values, block_table, ancestor_len, out_weight
):
    row_count = queries.shape[0]
    heads_here = queries.shape[1] // HD
    kv_here = new_keys.shape[1] // HD
    group_size = heads_here // kv_here
    slot_count = block_table.shape[1]
    score_scale = 1.0 / math.sqrt(HD)

    q = queries.reshape(row_count, kv_here, group_size, HD).transpose(1, 2, 0, 3)
    own_k = new_keys.reshape(row_count, kv_here, HD).transpose(1, 0, 2)
    own_v = new_values.reshape(row_count, kv_here, HD).transpose(1, 0, 2)

    kv_local = jnp.concatenate([cache_keys, cache_values], axis=-1)
    kv_chips = gather_by_all_to_all(kv_local, ("branch", "y", "zl"))
    n_core = lax.axis_size("core")
    kv_other = lax.ppermute(kv_chips, "core", [(c, (c + 1) % n_core) for c in range(n_core)])
    kv_all = jnp.concatenate([kv_chips, kv_other], axis=0)
    out_weight, kv_all = lax.optimization_barrier((out_weight, kv_all))
    w_cols = lax.all_gather(out_weight, ZC, axis=1, tiled=True)
    pages_here = cache_keys.shape[0]
    n_chips = lax.axis_size(("branch", "y", "zl"))
    owner = block_table[0] // pages_here
    other_core = (owner % n_core != lax.axis_index("core")).astype(jnp.int32)
    position = (other_core * n_chips + owner // n_core) * pages_here + block_table[0] % pages_here
    kv_sel = jnp.take(kv_all, position, axis=0)
    anc_len = slot_count * PAGE_TOK
    kv_sel = kv_sel.reshape(anc_len, 2, kv_here, HD)
    anc_k = kv_sel[:, 0].transpose(1, 0, 2)
    anc_v = kv_sel[:, 1].transpose(1, 0, 2)

    own_scores = (
        jnp.einsum("kgnd,kjd->kgnj", q, own_k, preferred_element_type=jnp.float32) * score_scale
    )
    anc_scores = (
        jnp.einsum("kgnd,kjd->kgnj", q, anc_k, preferred_element_type=jnp.float32) * score_scale
    )
    places = jnp.arange(row_count, dtype=jnp.int32)
    own_mask = places[None, :] <= places[:, None]
    anc_mask = jnp.arange(anc_len, dtype=jnp.int32) < ancestor_len[0]
    own_m = jnp.where(own_mask[None, None], own_scores, masked_fill)
    anc_m = jnp.where(anc_mask[None, None, None, :], anc_scores, masked_fill)
    row_max = jnp.maximum(jnp.max(own_m, axis=-1), jnp.max(anc_m, axis=-1))[..., None]
    own_w = jnp.where(own_mask[None, None], jnp.exp(own_scores - row_max), 0.0).astype(jnp.bfloat16)
    anc_w = jnp.where(anc_mask[None, None, None, :], jnp.exp(anc_scores - row_max), 0.0).astype(
        jnp.bfloat16
    )
    denom = jnp.sum(own_w.astype(jnp.float32), axis=-1) + jnp.sum(anc_w.astype(jnp.float32), axis=-1)
    summed = jnp.einsum(
        "kgnj,kjd->kgnd", own_w, own_v, preferred_element_type=jnp.float32
    ) + jnp.einsum("kgnj,kjd->kgnd", anc_w, anc_v, preferred_element_type=jnp.float32)
    attn = (summed / denom[..., None]).astype(jnp.bfloat16)
    attn_out = attn.transpose(2, 0, 1, 3).reshape(row_count, heads_here * HD)

    attn_rows = gather_by_all_to_all(attn_out, "y")
    partial_term = jnp.dot(attn_rows, w_cols, preferred_element_type=jnp.float32).astype(
        jnp.bfloat16
    )
    summed = lax.psum_scatter(partial_term, "head", scatter_dimension=0, tiled=True)
    n_zc = lax.axis_size(ZC)
    cols = out_weight.shape[1]
    summed = summed.reshape(row_count, n_zc, cols).transpose(1, 0, 2)
    arrived = lax.all_to_all(summed, ZC, 0, 0, tiled=True)
    return arrived.reshape(n_zc * row_count, cols)


def gather_by_all_to_all(x, axes):
    count = lax.axis_size(axes)
    spread = jnp.broadcast_to(x[None], (count,) + x.shape)
    arrived = lax.all_to_all(spread, axes, 0, 0, tiled=True)
    return arrived.reshape((count * x.shape[0],) + x.shape[1:])


PAGE_AXES = ("y", "zl", "core")
ZC = ("zl", "core")


def solution(mesh):
    n_page = mesh.shape["page"]
    n_core = 2
    n_y = 4
    fine = Mesh(
        np.asarray(mesh.devices).reshape(
            mesh.shape["branch"], mesh.shape["head"], n_y, n_page // (n_y * n_core), n_core
        ),
        ("branch", "head") + PAGE_AXES,
    )
    rows = ("branch",) + PAGE_AXES
    in_specs = (
        P(rows, "head"),
        P(rows, "head"),
        P(rows, "head"),
        P(rows, None, "head"),
        P(rows, None, "head"),
        P(rows, None),
        P(rows),
        P("head", PAGE_AXES),
    )
    out_specs = P(("branch", "head"), PAGE_AXES)
    return jax.shard_map(shards, mesh=fine, in_specs=in_specs, out_specs=out_specs, check_vma=False)
```

```python
import math

import jax
import jax.numpy as jnp
from jax import lax
from jax.sharding import Mesh
from jax.sharding import PartitionSpec as P
import numpy as np

HD = 128
PAGE_TOK = 64
NEW = 256


masked_fill = -1e30


def shards(
    queries, new_keys, new_values, cache_keys, cache_values, block_table, ancestor_len, out_weight
):
    row_count = queries.shape[0]
    heads_here = queries.shape[1] // HD
    kv_here = new_keys.shape[1] // HD
    group_size = heads_here // kv_here
    slot_count = block_table.shape[1]
    score_scale = 1.0 / math.sqrt(HD)

    q = queries.reshape(row_count, kv_here, group_size, HD).transpose(1, 2, 0, 3)
    own_k = new_keys.reshape(row_count, kv_here, HD).transpose(1, 0, 2)
    own_v = new_values.reshape(row_count, kv_here, HD).transpose(1, 0, 2)

    kv_local = jnp.concatenate([cache_keys, cache_values], axis=-1)
    kv_chips = gather_by_all_to_all(kv_local, ("branch", "y", "zl"))
    n_core = lax.axis_size("core")
    kv_other = lax.ppermute(kv_chips, "core", [(c, (c + 1) % n_core) for c in range(n_core)])
    kv_all = jnp.concatenate([kv_chips, kv_other], axis=0)
    out_weight, kv_all = lax.optimization_barrier((out_weight, kv_all))
    w_cols = lax.all_gather(out_weight, ZC, axis=1, tiled=True)
    pages_here = cache_keys.shape[0]
    n_chips = lax.axis_size(("branch", "y", "zl"))
    owner = block_table[0] // pages_here
    other_core = (owner % n_core != lax.axis_index("core")).astype(jnp.int32)
    position = (other_core * n_chips + owner // n_core) * pages_here + block_table[0] % pages_here
    kv_sel = jnp.take(kv_all, position, axis=0)
    anc_len = slot_count * PAGE_TOK
    kv_sel = kv_sel.reshape(anc_len, 2, kv_here, HD)
    anc_k = kv_sel[:, 0].transpose(1, 0, 2)
    anc_v = kv_sel[:, 1].transpose(1, 0, 2)

    own_scores = (
        jnp.einsum("kgnd,kjd->kgnj", q, own_k, preferred_element_type=jnp.float32) * score_scale
    )
    anc_scores = (
        jnp.einsum("kgnd,kjd->kgnj", q, anc_k, preferred_element_type=jnp.float32) * score_scale
    )
    places = jnp.arange(row_count, dtype=jnp.int32)
    own_mask = places[None, :] <= places[:, None]
    anc_mask = jnp.arange(anc_len, dtype=jnp.int32) < ancestor_len[0]
    own_m = jnp.where(own_mask[None, None], own_scores, masked_fill)
    anc_m = jnp.where(anc_mask[None, None, None, :], anc_scores, masked_fill)
    row_max = jnp.maximum(jnp.max(own_m, axis=-1), jnp.max(anc_m, axis=-1))[..., None]
    own_w = jnp.where(own_mask[None, None], jnp.exp(own_scores - row_max), 0.0).astype(jnp.bfloat16)
    anc_w = jnp.where(anc_mask[None, None, None, :], jnp.exp(anc_scores - row_max), 0.0).astype(
        jnp.bfloat16
    )
    denom = jnp.sum(own_w.astype(jnp.float32), axis=-1) + jnp.sum(anc_w.astype(jnp.float32), axis=-1)
    summed = jnp.einsum(
        "kgnj,kjd->kgnd", own_w, own_v, preferred_element_type=jnp.float32
    ) + jnp.einsum("kgnj,kjd->kgnd", anc_w, anc_v, preferred_element_type=jnp.float32)
    attn = (summed / denom[..., None]).astype(jnp.bfloat16)
    attn_out = attn.transpose(2, 0, 1, 3).reshape(row_count, heads_here * HD)

    attn_rows = gather_by_all_to_all(attn_out, "y")
    partial_term = jnp.dot(attn_rows, w_cols, preferred_element_type=jnp.float32).astype(
        jnp.bfloat16
    )
    summed = ring_reduce_scatter(partial_term, "head")
    n_zc = lax.axis_size(ZC)
    cols = out_weight.shape[1]
    summed = summed.reshape(row_count, n_zc, cols).transpose(1, 0, 2)
    arrived = lax.all_to_all(summed, ZC, 0, 0, tiled=True)
    return arrived.reshape(n_zc * row_count, cols)


def ring_reduce_scatter(x, axis):
    n = lax.axis_size(axis)
    i = lax.axis_index(axis)
    blocks = x.reshape(n, x.shape[0] // n, x.shape[1])
    half = x.shape[1] // 2
    ahead, behind = blocks[:, :, :half], blocks[:, :, half:]

    def block(part, offset):
        return lax.dynamic_index_in_dim(part, (i + offset + 2 * n) % n, axis=0, keepdims=False)

    forward = [(j, (j + 1) % n) for j in range(n)]
    backward = [(j, (j - 1) % n) for j in range(n)]
    up, down = block(ahead, -1), block(behind, 1)
    for step in range(n - 1):
        came_up = lax.ppermute(up, axis, forward)
        came_down = lax.ppermute(down, axis, backward)
        up = (came_up.astype(jnp.float32) + block(ahead, -step - 2).astype(jnp.float32)).astype(
            jnp.bfloat16
        )
        down = (came_down.astype(jnp.float32) + block(behind, step + 2).astype(jnp.float32)).astype(
            jnp.bfloat16
        )
    return jnp.concatenate([up, down], axis=1)


def gather_by_all_to_all(x, axes):
    count = lax.axis_size(axes)
    spread = jnp.broadcast_to(x[None], (count,) + x.shape)
    arrived = lax.all_to_all(spread, axes, 0, 0, tiled=True)
    return arrived.reshape((count * x.shape[0],) + x.shape[1:])


PAGE_AXES = ("y", "zl", "core")
ZC = ("zl", "core")


def solution(mesh):
    n_page = mesh.shape["page"]
    n_core = 2
    n_y = 4
    fine = Mesh(
        np.asarray(mesh.devices).reshape(
            mesh.shape["branch"], mesh.shape["head"], n_y, n_page // (n_y * n_core), n_core
        ),
        ("branch", "head") + PAGE_AXES,
    )
    rows = ("branch",) + PAGE_AXES
    in_specs = (
        P(rows, "head"),
        P(rows, "head"),
        P(rows, "head"),
        P(rows, None, "head"),
        P(rows, None, "head"),
        P(rows, None),
        P(rows),
        P("head", PAGE_AXES),
    )
    out_specs = P(("branch", "head"), PAGE_AXES)
    return jax.shard_map(shards, mesh=fine, in_specs=in_specs, out_specs=out_specs, check_vma=False)
```

```python
import math

import jax
import jax.numpy as jnp
from jax import lax
from jax.sharding import Mesh
from jax.sharding import PartitionSpec as P
import numpy as np

HD = 128
PAGE_TOK = 64
NEW = 256


masked_fill = -1e30


def shards(
    queries, new_keys, new_values, cache_keys, cache_values, block_table, ancestor_len, out_weight
):
    row_count = queries.shape[0]
    heads_here = queries.shape[1] // HD
    kv_here = new_keys.shape[1] // HD
    group_size = heads_here // kv_here
    slot_count = block_table.shape[1]
    score_scale = 1.0 / math.sqrt(HD)

    q = queries.reshape(row_count, kv_here, group_size, HD).transpose(1, 2, 0, 3)
    own_k = new_keys.reshape(row_count, kv_here, HD).transpose(1, 0, 2)
    own_v = new_values.reshape(row_count, kv_here, HD).transpose(1, 0, 2)

    kv_local = jnp.concatenate([cache_keys, cache_values], axis=-1)
    kv_chips = gather_by_all_to_all(kv_local, ("branch", "y", "zl"))
    n_core = lax.axis_size("core")
    pages_here = cache_keys.shape[0]
    swap = [(c, (c + 1) % n_core) for c in range(n_core)]
    partner_row = lax.ppermute(block_table, "core", swap)[0]
    partner_pos = (partner_row // pages_here // n_core) * pages_here + partner_row % pages_here
    from_partner = lax.ppermute(jnp.take(kv_chips, partner_pos, axis=0), "core", swap)
    own_row = block_table[0]
    owner = own_row // pages_here
    own_pos = (owner // n_core) * pages_here + own_row % pages_here
    other_core = owner % n_core != lax.axis_index("core")
    kv_sel = jnp.where(other_core[:, None, None], from_partner, jnp.take(kv_chips, own_pos, axis=0))
    out_weight, kv_sel = lax.optimization_barrier((out_weight, kv_sel))
    w_cols = lax.all_gather(out_weight, ZC, axis=1, tiled=True)
    anc_len = slot_count * PAGE_TOK
    kv_sel = kv_sel.reshape(anc_len, 2, kv_here, HD)
    anc_k = kv_sel[:, 0].transpose(1, 0, 2)
    anc_v = kv_sel[:, 1].transpose(1, 0, 2)

    own_scores = (
        jnp.einsum("kgnd,kjd->kgnj", q, own_k, preferred_element_type=jnp.float32) * score_scale
    )
    anc_scores = (
        jnp.einsum("kgnd,kjd->kgnj", q, anc_k, preferred_element_type=jnp.float32) * score_scale
    )
    places = jnp.arange(row_count, dtype=jnp.int32)
    own_mask = places[None, :] <= places[:, None]
    anc_mask = jnp.arange(anc_len, dtype=jnp.int32) < ancestor_len[0]
    own_m = jnp.where(own_mask[None, None], own_scores, masked_fill)
    anc_m = jnp.where(anc_mask[None, None, None, :], anc_scores, masked_fill)
    row_max = jnp.maximum(jnp.max(own_m, axis=-1), jnp.max(anc_m, axis=-1))[..., None]
    own_w = jnp.where(own_mask[None, None], jnp.exp(own_scores - row_max), 0.0).astype(jnp.bfloat16)
    anc_w = jnp.where(anc_mask[None, None, None, :], jnp.exp(anc_scores - row_max), 0.0).astype(
        jnp.bfloat16
    )
    denom = jnp.sum(own_w.astype(jnp.float32), axis=-1) + jnp.sum(anc_w.astype(jnp.float32), axis=-1)
    summed = jnp.einsum(
        "kgnj,kjd->kgnd", own_w, own_v, preferred_element_type=jnp.float32
    ) + jnp.einsum("kgnj,kjd->kgnd", anc_w, anc_v, preferred_element_type=jnp.float32)
    attn = (summed / denom[..., None]).astype(jnp.bfloat16)
    attn_out = attn.transpose(2, 0, 1, 3).reshape(row_count, heads_here * HD)

    attn_rows = gather_by_all_to_all(attn_out, "y")
    partial_term = jnp.dot(attn_rows, w_cols, preferred_element_type=jnp.float32).astype(
        jnp.bfloat16
    )
    summed = lax.psum_scatter(partial_term, "head", scatter_dimension=0, tiled=True)
    n_zc = lax.axis_size(ZC)
    cols = out_weight.shape[1]
    summed = summed.reshape(row_count, n_zc, cols).transpose(1, 0, 2)
    arrived = lax.all_to_all(summed, ZC, 0, 0, tiled=True)
    return arrived.reshape(n_zc * row_count, cols)


def gather_by_all_to_all(x, axes):
    count = lax.axis_size(axes)
    spread = jnp.broadcast_to(x[None], (count,) + x.shape)
    arrived = lax.all_to_all(spread, axes, 0, 0, tiled=True)
    return arrived.reshape((count * x.shape[0],) + x.shape[1:])


PAGE_AXES = ("y", "zl", "core")
ZC = ("zl", "core")


def solution(mesh):
    n_page = mesh.shape["page"]
    n_core = 2
    n_y = 4
    fine = Mesh(
        np.asarray(mesh.devices).reshape(
            mesh.shape["branch"], mesh.shape["head"], n_y, n_page // (n_y * n_core), n_core
        ),
        ("branch", "head") + PAGE_AXES,
    )
    rows = ("branch",) + PAGE_AXES
    in_specs = (
        P(rows, "head"),
        P(rows, "head"),
        P(rows, "head"),
        P(rows, None, "head"),
        P(rows, None, "head"),
        P(rows, None),
        P(rows),
        P("head", PAGE_AXES),
    )
    out_specs = P(("branch", "head"), PAGE_AXES)
    return jax.shard_map(shards, mesh=fine, in_specs=in_specs, out_specs=out_specs, check_vma=False)
```

```python
import math

import jax
import jax.numpy as jnp
from jax import lax
from jax.sharding import Mesh
from jax.sharding import PartitionSpec as P
import numpy as np

HD = 128
PAGE_TOK = 64
NEW = 256


masked_fill = -1e30


def shards(
    queries, new_keys, new_values, cache_keys, cache_values, block_table, ancestor_len, out_weight
):
    row_count = queries.shape[0]
    heads_here = queries.shape[1] // HD
    kv_here = new_keys.shape[1] // HD
    group_size = heads_here // kv_here
    slot_count = block_table.shape[1]
    score_scale = 1.0 / math.sqrt(HD)

    q = queries.reshape(row_count, kv_here, group_size, HD).transpose(1, 2, 0, 3)
    own_k = new_keys.reshape(row_count, kv_here, HD).transpose(1, 0, 2)
    own_v = new_values.reshape(row_count, kv_here, HD).transpose(1, 0, 2)

    kv_local = jnp.concatenate([cache_keys, cache_values], axis=-1)
    kv_chips = gather_by_all_to_all(kv_local, ("branch", "y", "zl"))
    out_weight, kv_chips = lax.optimization_barrier((out_weight, kv_chips))
    w_cols = lax.all_gather(out_weight, ZC, axis=1, tiled=True)
    n_core = lax.axis_size("core")
    kv_other = lax.ppermute(kv_chips, "core", [(c, (c + 1) % n_core) for c in range(n_core)])
    kv_all = jnp.concatenate([kv_chips, kv_other], axis=0)
    pages_here = cache_keys.shape[0]
    n_chips = lax.axis_size(("branch", "y", "zl"))
    owner = block_table[0] // pages_here
    other_core = (owner % n_core != lax.axis_index("core")).astype(jnp.int32)
    position = (other_core * n_chips + owner // n_core) * pages_here + block_table[0] % pages_here
    kv_sel = jnp.take(kv_all, position, axis=0)
    anc_len = slot_count * PAGE_TOK
    kv_sel = kv_sel.reshape(anc_len, 2, kv_here, HD)
    anc_k = kv_sel[:, 0].transpose(1, 0, 2)
    anc_v = kv_sel[:, 1].transpose(1, 0, 2)

    own_scores = (
        jnp.einsum("kgnd,kjd->kgnj", q, own_k, preferred_element_type=jnp.float32) * score_scale
    )
    anc_scores = (
        jnp.einsum("kgnd,kjd->kgnj", q, anc_k, preferred_element_type=jnp.float32) * score_scale
    )
    places = jnp.arange(row_count, dtype=jnp.int32)
    own_mask = places[None, :] <= places[:, None]
    anc_mask = jnp.arange(anc_len, dtype=jnp.int32) < ancestor_len[0]
    own_m = jnp.where(own_mask[None, None], own_scores, masked_fill)
    anc_m = jnp.where(anc_mask[None, None, None, :], anc_scores, masked_fill)
    row_max = jnp.maximum(jnp.max(own_m, axis=-1), jnp.max(anc_m, axis=-1))[..., None]
    own_w = jnp.where(own_mask[None, None], jnp.exp(own_scores - row_max), 0.0).astype(jnp.bfloat16)
    anc_w = jnp.where(anc_mask[None, None, None, :], jnp.exp(anc_scores - row_max), 0.0).astype(
        jnp.bfloat16
    )
    denom = jnp.sum(own_w.astype(jnp.float32), axis=-1) + jnp.sum(anc_w.astype(jnp.float32), axis=-1)
    summed = jnp.einsum(
        "kgnj,kjd->kgnd", own_w, own_v, preferred_element_type=jnp.float32
    ) + jnp.einsum("kgnj,kjd->kgnd", anc_w, anc_v, preferred_element_type=jnp.float32)
    attn = (summed / denom[..., None]).astype(jnp.bfloat16)
    attn_out = attn.transpose(2, 0, 1, 3).reshape(row_count, heads_here * HD)

    attn_rows = gather_by_all_to_all(attn_out, "y")
    partial_term = jnp.dot(attn_rows, w_cols, preferred_element_type=jnp.float32).astype(
        jnp.bfloat16
    )
    summed = lax.psum_scatter(partial_term, "head", scatter_dimension=0, tiled=True)
    n_zc = lax.axis_size(ZC)
    cols = out_weight.shape[1]
    summed = summed.reshape(row_count, n_zc, cols).transpose(1, 0, 2)
    arrived = lax.all_to_all(summed, ZC, 0, 0, tiled=True)
    return arrived.reshape(n_zc * row_count, cols)


def gather_by_all_to_all(x, axes):
    count = lax.axis_size(axes)
    spread = jnp.broadcast_to(x[None], (count,) + x.shape)
    arrived = lax.all_to_all(spread, axes, 0, 0, tiled=True)
    return arrived.reshape((count * x.shape[0],) + x.shape[1:])


PAGE_AXES = ("y", "zl", "core")
ZC = ("zl", "core")


def solution(mesh):
    n_page = mesh.shape["page"]
    n_core = 2
    n_y = 4
    fine = Mesh(
        np.asarray(mesh.devices).reshape(
            mesh.shape["branch"], mesh.shape["head"], n_y, n_page // (n_y * n_core), n_core
        ),
        ("branch", "head") + PAGE_AXES,
    )
    rows = ("branch",) + PAGE_AXES
    in_specs = (
        P(rows, "head"),
        P(rows, "head"),
        P(rows, "head"),
        P(rows, None, "head"),
        P(rows, None, "head"),
        P(rows, None),
        P(rows),
        P("head", PAGE_AXES),
    )
    out_specs = P(("branch", "head"), PAGE_AXES)
    return jax.shard_map(shards, mesh=fine, in_specs=in_specs, out_specs=out_specs, check_vma=False)
```
